128 devices in a mesh: hid: 4 (over y), wid: 32 (over z, x, core).
Axes of the slice: x: 4, y: 4, z: 4, core: 2. Of those that a mesh axis runs over, the one named last changes fastest.
Arguments:
- tokens: bfloat16 [512, 16384], P(None, 'wid'), may hold values from -6 to 6
- gate_quant: bfloat16 [16384, 26624], P('wid', 'hid'), may hold values from -0.046875 to 0.046875
- gate_scale: float32 [128, 208], P('wid', 'hid'), may hold values from 0.25 to 4
- up_quant: bfloat16 [16384, 26624], P('wid', 'hid'), may hold values from -0.046875 to 0.046875
- up_scale: float32 [128, 208], P('wid', 'hid'), may hold values from 0.25 to 4
- down_quant: bfloat16 [26624, 16384], P('hid', 'wid'), may hold values from -0.0390625 to 0.0390625
- down_scale: float32 [208, 128], P('hid', 'wid'), may hold values from 0.25 to 4
Outputs:
- mixed: bfloat16 [512, 16384], P(None, 'wid')
The draws below stay inside these ranges and needn't reach their ends.
All inputs are finite; a program needn't handle non-finite values.
Results may differ from the reference program's by a relative error of at most 0.03.
Values may be sent and summed in bfloat16 or wider, within the bound.
No kernel may reach another device: no remote copies, remote signals or barrier semaphores. Data moves between devices by JAX's collectives and lax.ppermute only.
A program may use at most 128 MiB of HBM per device.

```python
import math
import jax
import jax.numpy as jnp
from jax import lax

D = 16384
FFW = 26624
BLK = 128
ROWS = 512
N_WID = 32


def block_scale(stream_key, shape, shards, smallest, largest):
    def one(dim, shards_of):
        heights = jax.random.uniform(jax.random.fold_in(jax.random.fold_in(stream_key, 6), dim), (shards_of,), jnp.float32, smallest / len(shards), largest / len(shards))
        return jnp.repeat(jnp.exp(heights), shape[dim] // shards_of).reshape((-1,) + (1,) * (len(shape) - dim - 1))

    loudness = one(*shards[0])
    for cut in shards[1:]:
        loudness = loudness * one(*cut)
    return loudness


def normal_values(rng, shape, spread, limit, split=(), held_as=jnp.bfloat16):
    result = spread * jax.random.normal(rng, shape, jnp.float32)
    if split:
        result = result * block_scale(rng, shape, split, -0.22, 0.18)
    return jnp.clip(result, -limit, limit).astype(held_as)


def setup_inputs(seed: int = 0) -> dict:
    seeds = jax.random.split(jax.random.key(seed), 8)
    tokens = normal_values(seeds[0], (ROWS, D), 1.0, 6.0, ((1, 32),))
    gate_quant = normal_values(seeds[1], (D, FFW), D ** -0.5, 0.046875, ((0, 32), (1, 4)))
    gate_scale = jnp.clip(jnp.exp(math.log(4.0) - 2.7725887 * jax.random.uniform(seeds[2], (D // BLK, FFW // BLK), jnp.float32) ** block_scale(seeds[2], (D // BLK, FFW // BLK), ((0, 32), (1, 4)), -0.2, 0.2)), 0.25, 4.0)
    up_quant = normal_values(seeds[3], (D, FFW), D ** -0.5, 0.046875, ((0, 32), (1, 4)))
    up_scale = jnp.clip(jnp.exp(math.log(4.0) - 2.7725887 * jax.random.uniform(seeds[4], (D // BLK, FFW // BLK), jnp.float32) ** block_scale(seeds[4], (D // BLK, FFW // BLK), ((0, 32), (1, 4)), -0.2, 0.2)), 0.25, 4.0)
    down_quant = normal_values(seeds[5], (FFW, D), FFW ** -0.5, 0.0390625, ((0, 4), (1, 32)))
    down_scale = jnp.clip(jnp.exp(math.log(4.0) - 2.7725887 * jax.random.uniform(seeds[6], (FFW // BLK, D // BLK), jnp.float32) ** block_scale(seeds[6], (FFW // BLK, D // BLK), ((0, 4), (1, 32)), -0.2, 0.2)), 0.25, 4.0)
    return dict(tokens=tokens, gate_quant=gate_quant, gate_scale=gate_scale, up_quant=up_quant, up_scale=up_scale, down_quant=down_quant, down_scale=down_scale)


def dequant(quant, scale):
    rows, cols = quant.shape
    blocks = quant.astype(jnp.float32).reshape(rows // BLK, BLK, cols // BLK, BLK)
    return (blocks * scale[:, None, :, None]).reshape(rows, cols).astype(jnp.bfloat16)


def reference(tokens, gate_quant, gate_scale, up_quant, up_scale, down_quant, down_scale):
    width = D // N_WID

    def add_block(index, sums):
        gate_sum, up_sum = sums
        start = (index * width).astype(jnp.int32)
        rows_in = lax.dynamic_slice_in_dim(tokens, start, width, 1)
        gate_w = dequant(lax.dynamic_slice_in_dim(gate_quant, start, width, 0), lax.dynamic_slice_in_dim(gate_scale, start // BLK, width // BLK, 0))
        up_w = dequant(lax.dynamic_slice_in_dim(up_quant, start, width, 0), lax.dynamic_slice_in_dim(up_scale, start // BLK, width // BLK, 0))
        gate_part = jnp.dot(rows_in, gate_w, preferred_element_type=jnp.float32).astype(jnp.bfloat16)
        up_part = jnp.dot(rows_in, up_w, preferred_element_type=jnp.float32).astype(jnp.bfloat16)
        return (gate_sum + gate_part.astype(jnp.float32), up_sum + up_part.astype(jnp.float32))

    empty = jnp.zeros((ROWS, FFW), jnp.float32)
    gate, up = lax.fori_loop(0, N_WID, add_block, (empty, empty))
    hidden = (jax.nn.silu(gate) * up).astype(jnp.bfloat16)
    down_w = dequant(down_quant, down_scale)
    return jnp.dot(hidden, down_w, preferred_element_type=jnp.float32).astype(jnp.bfloat16)
```

```python
import functools

import jax
import jax.numpy as jnp
from jax import lax
from jax.experimental import pallas as pl
from jax.experimental.pallas import tpu as pltpu
from jax.sharding import PartitionSpec as P

BLK = 128
NZ, NX, NC = 4, 4, 2
GROUPS = 4
USE_PALLAS = True


def wid_of(z, x, c):
    return (z * NX + x) * NC + c


def perm_core():
    return [(wid_of(z, x, c), wid_of(z, x, 1 - c)) for z in range(NZ) for x in range(NX) for c in range(NC)]


def perm_x(d):
    return [(wid_of(z, x, c), wid_of(z, (x + d) % NX, c)) for z in range(NZ) for x in range(NX) for c in range(NC)]


def perm_z(d):
    return [(wid_of(z, x, c), wid_of((z + d) % NZ, x, c)) for z in range(NZ) for x in range(NX) for c in range(NC)]


def perm_hid(n, d):
    return [(h, (h + d) % n) for h in range(n)]


def ring_rs(arr, axis, pos, perm, d, n):
    def own(j):
        return lax.dynamic_index_in_dim(arr, j, axis, keepdims=False).astype(jnp.float32)

    send = own((pos - d) % n)
    acc = None
    for s in range(n - 1):
        recv = lax.ppermute(send.astype(jnp.bfloat16), "wid", perm).astype(jnp.float32)
        acc = recv + own((pos - d * (s + 2)) % n)
        send = acc
    return acc


def ring_ag(chunk, axis, pos, perm, d, n):
    shape = list(chunk.shape)
    shape.insert(axis, n)
    out = jnp.zeros(shape, chunk.dtype)

    def put(o, c, j):
        starts = [0] * len(shape)
        starts[axis] = j
        return lax.dynamic_update_slice(o, jnp.expand_dims(c, axis), starts)

    out = put(out, chunk, pos)
    send = chunk
    for s in range(n - 1):
        recv = lax.ppermute(send, "wid", perm)
        out = put(out, recv, (pos - d * (s + 1)) % n)
        send = recv
    return out


def gate_up_kernel(t_ref, gq_ref, gs_ref, uq_ref, us_ref, go_ref, uo_ref):
    t = t_ref[...]
    kb = t_ref.shape[1] // BLK
    for q_ref, s_ref, o_ref in ((gq_ref, gs_ref, go_ref), (uq_ref, us_ref, uo_ref)):
        parts = []
        for b in range(kb):
            qb = q_ref[b * BLK:(b + 1) * BLK, :].astype(jnp.float32)
            parts.append((qb * s_ref[b:b + 1, :]).astype(jnp.bfloat16))
        w = jnp.concatenate(parts, axis=0)
        o_ref[...] = jnp.dot(t, w, preferred_element_type=jnp.float32).astype(o_ref.dtype)


def gate_up(tokens, gq, gs, uq, us):
    rows, k = tokens.shape
    cols = gq.shape[1]
    gsr = jnp.repeat(gs, BLK, axis=1)
    usr = jnp.repeat(us, BLK, axis=1)
    if not USE_PALLAS:
        def deq(q, sr):
            return (q.astype(jnp.float32) * jnp.repeat(sr, BLK, axis=0)).astype(jnp.bfloat16)
        g = jnp.dot(tokens, deq(gq, gsr), preferred_element_type=jnp.float32).astype(jnp.bfloat16)
        u = jnp.dot(tokens, deq(uq, usr), preferred_element_type=jnp.float32).astype(jnp.bfloat16)
        return g, u
    tn = 512
    nb = k // BLK
    return pl.pallas_call(
        gate_up_kernel,
        grid=(cols // tn,),
        in_specs=[
            pl.BlockSpec((rows, k), lambda j: (0, 0)),
            pl.BlockSpec((k, tn), lambda j: (0, j)),
            pl.BlockSpec((nb, tn), lambda j: (0, j)),
            pl.BlockSpec((k, tn), lambda j: (0, j)),
            pl.BlockSpec((nb, tn), lambda j: (0, j)),
        ],
        out_specs=[
            pl.BlockSpec((rows, tn), lambda j: (0, j)),
            pl.BlockSpec((rows, tn), lambda j: (0, j)),
        ],
        out_shape=[
            jax.ShapeDtypeStruct((rows, cols), jnp.bfloat16),
            jax.ShapeDtypeStruct((rows, cols), jnp.bfloat16),
        ],
    )(tokens, gq, gsr, uq, usr)


def down_kernel(h_ref, q_ref, s_ref, o_ref, acc_ref):
    k = pl.program_id(0)
    tk = q_ref.shape[0]
    nb = tk // BLK

    @pl.when(k == 0)
    def _():
        acc_ref[...] = jnp.zeros_like(acc_ref)

    parts = []
    for b in range(nb):
        qb = q_ref[b * BLK:(b + 1) * BLK, :].astype(jnp.float32)
        sb = s_ref[pl.ds(k * nb + b, 1), :]
        parts.append((qb * sb).astype(jnp.bfloat16))
    w = jnp.concatenate(parts, axis=0)
    acc_ref[...] += jnp.dot(h_ref[...], w, preferred_element_type=jnp.float32)

    @pl.when(k == pl.num_programs(0) - 1)
    def _():
        o_ref[...] = acc_ref[...]


def down(hidden, dq, ds):
    rows, kdim = hidden.shape
    cols = dq.shape[1]
    dsr = jnp.repeat(ds, BLK, axis=1)
    if not USE_PALLAS:
        w = (dq.astype(jnp.float32) * jnp.repeat(dsr, BLK, axis=0)).astype(jnp.bfloat16)
        return jnp.dot(hidden, w, preferred_element_type=jnp.float32)
    tk = 1664
    return pl.pallas_call(
        down_kernel,
        grid=(kdim // tk,),
        in_specs=[
            pl.BlockSpec((rows, tk), lambda k: (0, k)),
            pl.BlockSpec((tk, cols), lambda k: (k, 0)),
            pl.BlockSpec(dsr.shape, lambda k: (0, 0)),
        ],
        out_specs=pl.BlockSpec((rows, cols), lambda k: (0, 0)),
        out_shape=jax.ShapeDtypeStruct((rows, cols), jnp.float32),
        scratch_shapes=[pltpu.VMEM((rows, cols), jnp.float32)],
    )(hidden, dq, dsr)


def shards(n_hid, tokens, gate_quant, gate_scale, up_quant, up_scale, down_quant, down_scale):
    w = lax.axis_index("wid")
    c = w % NC
    x = (w // NC) % NX
    z = w // (NC * NX)
    rows = tokens.shape[0]
    cols = gate_quant.shape[1]
    half = cols // NC
    blk = half // (NX * NZ)
    gr = rows // GROUPS

    g, u = gate_up(tokens, gate_quant, gate_scale, up_quant, up_scale)
    both = jnp.stack([g, u])

    pc = perm_core()
    mine = lax.dynamic_slice_in_dim(both, c * half, half, axis=2)
    other = lax.dynamic_slice_in_dim(both, (1 - c) * half, half, axis=2)

    hid_parts = []
    for gi in range(GROUPS):
        rs = slice(gi * gr, (gi + 1) * gr)
        recv = lax.ppermute(other[:, rs], "wid", pc)
        q = mine[:, rs].astype(jnp.float32) + recv.astype(jnp.float32)
        qv = q.reshape(2, gr, NX, NZ, blk)
        d = 1 if gi % 2 == 0 else -1
        if gi < 2:
            r1 = ring_rs(qv, 2, x, perm_x(d), d, NX)
            r2 = ring_rs(r1, 2, z, perm_z(d), d, NZ)
        else:
            r1 = ring_rs(qv, 3, z, perm_z(d), d, NZ)
            r2 = ring_rs(r1, 2, x, perm_x(d), d, NX)
        hg = (jax.nn.silu(r2[0]) * r2[1]).astype(jnp.bfloat16)
        if gi < 2:
            a1 = ring_ag(hg, 1, z, perm_z(d), d, NZ)
            a2 = ring_ag(a1, 1, x, perm_x(d), d, NX)
        else:
            a1 = ring_ag(hg, 1, x, perm_x(d), d, NX)
            a2 = ring_ag(a1, 2, z, perm_z(d), d, NZ)
        hmine = a2.reshape(gr, half)
        hother = lax.ppermute(hmine, "wid", pc)
        full = jnp.zeros((gr, cols), jnp.bfloat16)
        full = lax.dynamic_update_slice(full, hmine, (0, c * half))
        full = lax.dynamic_update_slice(full, hother, (0, (1 - c) * half))
        hid_parts.append(full)
    hidden = jnp.concatenate(hid_parts, axis=0)

    pout = down(hidden, down_quant, down_scale)
    pb = pout.astype(jnp.bfloat16)
    from_minus = lax.ppermute(pb, "hid", perm_hid(n_hid, 1))
    from_plus = lax.ppermute(pb, "hid", perm_hid(n_hid, -1))
    hr = rows // 2
    fwd_a = lax.ppermute(from_minus[:hr], "hid", perm_hid(n_hid, 1))
    fwd_b = lax.ppermute(from_plus[hr:], "hid", perm_hid(n_hid, -1))
    far = jnp.concatenate([fwd_a, fwd_b], axis=0).astype(jnp.float32)
    total = pout + from_minus.astype(jnp.float32) + from_plus.astype(jnp.float32) + far
    return total.astype(jnp.bfloat16)


def solution(mesh):
    n_hid = mesh.shape["hid"]
    assert n_hid == 4 and mesh.shape["wid"] == NZ * NX * NC
    return jax.shard_map(
        functools.partial(shards, n_hid),
        mesh=mesh,
        in_specs=(
            P(None, "wid"),
            P("wid", "hid"),
            P("wid", "hid"),
            P("wid", "hid"),
            P("wid", "hid"),
            P("hid", "wid"),
            P("hid", "wid"),
        ),
        out_specs=P(None, "wid"),
        check_vma=False,
    )
```

```python
import functools

import jax
import jax.numpy as jnp
from jax import lax
from jax.experimental import pallas as pl
from jax.experimental.pallas import tpu as pltpu
from jax.sharding import PartitionSpec as P

BLK = 128
NZ, NX, NC = 4, 4, 2
GROUPS = 4
USE_PALLAS = True


def wid_of(z, x, c):
    return (z * NX + x) * NC + c


def perm_core():
    return [(wid_of(z, x, c), wid_of(z, x, 1 - c)) for z in range(NZ) for x in range(NX) for c in range(NC)]


def perm_x(d):
    return [(wid_of(z, x, c), wid_of(z, (x + d) % NX, c)) for z in range(NZ) for x in range(NX) for c in range(NC)]


def perm_z(d):
    return [(wid_of(z, x, c), wid_of((z + d) % NZ, x, c)) for z in range(NZ) for x in range(NX) for c in range(NC)]


def perm_hid(n, d):
    return [(h, (h + d) % n) for h in range(n)]


def ring_rs(arr, axis, pos, perm, d, n):
    size = arr.shape[axis] // n

    def own(j):
        return lax.dynamic_slice_in_dim(arr, j * size, size, axis).astype(jnp.float32)

    send = own((pos - d) % n)
    acc = None
    for s in range(n - 1):
        recv = lax.ppermute(send.astype(jnp.bfloat16), "wid", perm).astype(jnp.float32)
        acc = recv + own((pos - d * (s + 2)) % n)
        send = acc
    return acc


def ring_ag(chunk, pos, perm, d, n):
    rows = chunk.shape[0]
    out = jnp.zeros((n * rows,) + chunk.shape[1:], chunk.dtype)

    def put(o, c, j):
        return lax.dynamic_update_slice_in_dim(o, c, j * rows, 0)

    out = put(out, chunk, pos)
    send = chunk
    for s in range(n - 1):
        recv = lax.ppermute(send, "wid", perm)
        out = put(out, recv, (pos - d * (s + 1)) % n)
        send = recv
    return out


def gate_up_kernel(t_ref, gq_ref, gs_ref, uq_ref, us_ref, o_ref):
    t = t_ref[...]
    kb = t_ref.shape[1] // BLK
    half = o_ref.shape[3]
    for gi, (q_ref, s_ref) in enumerate(((gq_ref, gs_ref), (uq_ref, us_ref))):
        parts = []
        for b in range(kb):
            qb = q_ref[b * BLK:(b + 1) * BLK, :].astype(jnp.float32)
            parts.append((qb * s_ref[b:b + 1, :]).astype(jnp.bfloat16))
        w = jnp.concatenate(parts, axis=0)
        res = jnp.dot(t, w, preferred_element_type=jnp.float32).astype(o_ref.dtype)
        for h in range(2):
            o_ref[h, 0, gi] = res[h * half:(h + 1) * half]


def gate_up(tokens, gq, gs, uq, us):
    rows, k = tokens.shape
    cols = gq.shape[1]
    tn = cols // GROUPS
    hr = rows // 2
    gsr = jnp.repeat(gs, BLK, axis=1)
    usr = jnp.repeat(us, BLK, axis=1)
    if not USE_PALLAS:
        def deq(q, sr):
            return (q.astype(jnp.float32) * jnp.repeat(sr, BLK, axis=0)).astype(jnp.bfloat16)
        g = jnp.dot(tokens, deq(gq, gsr), preferred_element_type=jnp.float32).astype(jnp.bfloat16)
        u = jnp.dot(tokens, deq(uq, usr), preferred_element_type=jnp.float32).astype(jnp.bfloat16)
        both = jnp.stack([g, u])
        both = both.reshape(2, 2, hr, GROUPS, tn)
        return both.transpose(1, 3, 0, 2, 4)
    nb = k // BLK
    return pl.pallas_call(
        gate_up_kernel,
        grid=(GROUPS,),
        in_specs=[
            pl.BlockSpec((rows, k), lambda j: (0, 0)),
            pl.BlockSpec((k, tn), lambda j: (0, j)),
            pl.BlockSpec((nb, tn), lambda j: (0, j)),
            pl.BlockSpec((k, tn), lambda j: (0, j)),
            pl.BlockSpec((nb, tn), lambda j: (0, j)),
        ],
        out_specs=pl.BlockSpec((2, 1, 2, hr, tn), lambda j: (0, j, 0, 0, 0)),
        out_shape=jax.ShapeDtypeStruct((2, GROUPS, 2, hr, tn), jnp.bfloat16),
        compiler_params=pltpu.CompilerParams(vmem_limit_bytes=48 * 1024 * 1024),
    )(tokens, gq, gsr, uq, usr)


def down_kernel(h_ref, q_ref, s_ref, o_ref):
    k = pl.program_id(0)
    tk = q_ref.shape[0]
    nb = tk // BLK

    @pl.when(k == 0)
    def _():
        o_ref[...] = jnp.zeros_like(o_ref)

    parts = []
    for b in range(nb):
        qb = q_ref[b * BLK:(b + 1) * BLK, :].astype(jnp.float32)
        sb = s_ref[pl.ds(k * nb + b, 1), :]
        parts.append((qb * sb).astype(jnp.bfloat16))
    w = jnp.concatenate(parts, axis=0)
    o_ref[...] += jnp.dot(h_ref[0], w, preferred_element_type=jnp.float32)


def down(hidden, dq, dsr):
    groups, rows, tk = hidden.shape
    cols = dq.shape[1]
    if not USE_PALLAS:
        w = (dq.astype(jnp.float32) * jnp.repeat(dsr, BLK, axis=0)).astype(jnp.bfloat16)
        h = hidden.transpose(1, 0, 2).reshape(rows, groups * tk)
        return jnp.dot(h, w, preferred_element_type=jnp.float32)
    return pl.pallas_call(
        down_kernel,
        grid=(groups,),
        in_specs=[
            pl.BlockSpec((1, rows, tk), lambda k: (k, 0, 0)),
            pl.BlockSpec((tk, cols), lambda k: (k, 0)),
            pl.BlockSpec(dsr.shape, lambda k: (0, 0)),
        ],
        out_specs=pl.BlockSpec((rows, cols), lambda k: (0, 0)),
        out_shape=jax.ShapeDtypeStruct((rows, cols), jnp.float32),
    )(hidden, dq, dsr)


def hid_sum(pout, n_hid):
    pb = pout.astype(jnp.bfloat16)
    from_minus = lax.ppermute(pb, "hid", perm_hid(n_hid, 1))
    from_plus = lax.ppermute(pb, "hid", perm_hid(n_hid, -1))
    hr = pout.shape[0] // 2
    fwd_a = lax.ppermute(from_minus[:hr], "hid", perm_hid(n_hid, 1))
    fwd_b = lax.ppermute(from_plus[hr:], "hid", perm_hid(n_hid, -1))
    far = jnp.concatenate([fwd_a, fwd_b], axis=0).astype(jnp.float32)
    return pout + from_minus.astype(jnp.float32) + from_plus.astype(jnp.float32) + far


def shards(n_hid, tokens, gate_quant, gate_scale, up_quant, up_scale, down_quant, down_scale):
    w = lax.axis_index("wid")
    c = w % NC
    x = (w // NC) % NX
    z = w // (NC * NX)
    rows = tokens.shape[0]
    hr = rows // 2

    tok = jnp.concatenate([tokens, tokens], axis=0)
    tok = lax.dynamic_slice_in_dim(tok, c * hr, rows, 0)
    out = gate_up(tok, gate_quant, gate_scale, up_quant, up_scale)

    pc = perm_core()
    hmine, hother = [], []
    for gi in range(GROUPS):
        recv = lax.ppermute(out[1, gi], "wid", pc)
        q = out[0, gi].astype(jnp.float32) + recv.astype(jnp.float32)
        d = 1 if gi % 2 == 0 else -1
        if gi < 2:
            r1 = ring_rs(q, 1, x, perm_x(d), d, NX)
            r2 = ring_rs(r1, 1, z, perm_z(d), d, NZ)
        else:
            r1 = ring_rs(q, 1, z, perm_z(d), d, NZ)
            r2 = ring_rs(r1, 1, x, perm_x(d), d, NX)
        hg = (jax.nn.silu(r2[0]) * r2[1]).astype(jnp.bfloat16)
        if gi < 2:
            a1 = ring_ag(hg, z, perm_z(d), d, NZ)
            a2 = ring_ag(a1, x, perm_x(d), d, NX)
        else:
            a1 = ring_ag(hg, x, perm_x(d), d, NX)
            a2 = ring_ag(a1, z, perm_z(d), d, NZ)
        hmine.append(a2)
        hother.append(lax.ppermute(a2, "wid", pc))

    dsr = jnp.repeat(down_scale, BLK, axis=1)
    p_mine = down(jnp.stack(hmine), down_quant, dsr)
    s_mine = hid_sum(p_mine, n_hid)
    p_other = down(jnp.stack(hother), down_quant, dsr)
    s_other = hid_sum(p_other, n_hid)
    rolled = jnp.concatenate([s_mine, s_other, s_mine], axis=0).astype(jnp.bfloat16)
    return lax.dynamic_slice_in_dim(rolled, c * hr, rows, 0)


def solution(mesh):
    n_hid = mesh.shape["hid"]
    assert n_hid == 4 and mesh.shape["wid"] == NZ * NX * NC
    return jax.shard_map(
        functools.partial(shards, n_hid),
        mesh=mesh,
        in_specs=(
            P(None, "wid"),
            P("wid", "hid"),
            P("wid", "hid"),
            P("wid", "hid"),
            P("wid", "hid"),
            P("hid", "wid"),
            P("hid", "wid"),
        ),
        out_specs=P(None, "wid"),
        check_vma=False,
    )
```

```python
import functools

import jax
import jax.numpy as jnp
from jax import lax
from jax.experimental import pallas as pl
from jax.experimental.pallas import tpu as pltpu
from jax.sharding import PartitionSpec as P

BLK = 128
NZ, NX, NC = 4, 4, 2
GROUPS = 4
USE_PALLAS = True


def wid_of(z, x, c):
    return (z * NX + x) * NC + c


def perm_core():
    return [(wid_of(z, x, c), wid_of(z, x, 1 - c)) for z in range(NZ) for x in range(NX) for c in range(NC)]


def perm_x(d):
    return [(wid_of(z, x, c), wid_of(z, (x + d) % NX, c)) for z in range(NZ) for x in range(NX) for c in range(NC)]


def perm_z(d):
    return [(wid_of(z, x, c), wid_of((z + d) % NZ, x, c)) for z in range(NZ) for x in range(NX) for c in range(NC)]


def perm_hid(n, d):
    return [(h, (h + d) % n) for h in range(n)]


def ring_rs(arr, axis, pos, perm, d, n):
    size = arr.shape[axis] // n

    def own(j):
        return lax.dynamic_slice_in_dim(arr, j * size, size, axis).astype(jnp.float32)

    send = own((pos - d) % n)
    acc = None
    for s in range(n - 1):
        recv = lax.ppermute(send.astype(jnp.bfloat16), "wid", perm).astype(jnp.float32)
        acc = recv + own((pos - d * (s + 2)) % n)
        send = acc
    return acc


def ring_ag(chunk, pos, perm, d, n):
    rows = chunk.shape[0]
    out = jnp.zeros((n * rows,) + chunk.shape[1:], chunk.dtype)

    def put(o, c, j):
        return lax.dynamic_update_slice_in_dim(o, c, j * rows, 0)

    out = put(out, chunk, pos)
    send = chunk
    for s in range(n - 1):
        recv = lax.ppermute(send, "wid", perm)
        out = put(out, recv, (pos - d * (s + 1)) % n)
        send = recv
    return out


def direct_rs(arr, axis, pos, perm_of, n):
    size = arr.shape[axis] // n

    def own(j):
        return lax.dynamic_slice_in_dim(arr, j * size, size, axis)

    acc = own(pos).astype(jnp.float32)
    for o in range(1, n):
        recv = lax.ppermute(own((pos + o) % n).astype(jnp.bfloat16), "wid", perm_of(o))
        acc = acc + recv.astype(jnp.float32)
    return acc


def direct_ag(chunk, pos, perm_of, n):
    rows = chunk.shape[0]
    out = jnp.zeros((n * rows,) + chunk.shape[1:], chunk.dtype)
    out = lax.dynamic_update_slice_in_dim(out, chunk, pos * rows, 0)
    for o in range(1, n):
        recv = lax.ppermute(chunk, "wid", perm_of(o))
        out = lax.dynamic_update_slice_in_dim(out, recv, ((pos - o) % n) * rows, 0)
    return out


def gate_up_kernel(t_ref, gq_ref, gs_ref, uq_ref, us_ref, o_ref):
    t = t_ref[...]
    kb = t_ref.shape[1] // BLK
    half = o_ref.shape[3]
    for gi, (q_ref, s_ref) in enumerate(((gq_ref, gs_ref), (uq_ref, us_ref))):
        parts = []
        for b in range(kb):
            qb = q_ref[b * BLK:(b + 1) * BLK, :].astype(jnp.float32)
            parts.append((qb * s_ref[b:b + 1, :]).astype(jnp.bfloat16))
        w = jnp.concatenate(parts, axis=0)
        res = jnp.dot(t, w, preferred_element_type=jnp.float32).astype(o_ref.dtype)
        for h in range(2):
            o_ref[h, 0, gi] = res[h * half:(h + 1) * half]


def gate_up(tokens, gq, gsr, uq, usr, gi):
    rows, k = tokens.shape
    cols = gq.shape[1]
    tn = cols // GROUPS
    hr = rows // 2
    if not USE_PALLAS:
        def deq(q, sr):
            q = q[:, gi * tn:(gi + 1) * tn]
            sr = sr[:, gi * tn:(gi + 1) * tn]
            return (q.astype(jnp.float32) * jnp.repeat(sr, BLK, axis=0)).astype(jnp.bfloat16)
        g = jnp.dot(tokens, deq(gq, gsr), preferred_element_type=jnp.float32).astype(jnp.bfloat16)
        u = jnp.dot(tokens, deq(uq, usr), preferred_element_type=jnp.float32).astype(jnp.bfloat16)
        both = jnp.stack([g, u])
        return both.reshape(2, 2, hr, tn).transpose(1, 0, 2, 3)[:, None]
    nb = k // BLK
    return pl.pallas_call(
        gate_up_kernel,
        grid=(1,),
        in_specs=[
            pl.BlockSpec((rows, k), lambda j: (0, 0)),
            pl.BlockSpec((k, tn), lambda j: (0, gi)),
            pl.BlockSpec((nb, tn), lambda j: (0, gi)),
            pl.BlockSpec((k, tn), lambda j: (0, gi)),
            pl.BlockSpec((nb, tn), lambda j: (0, gi)),
        ],
        out_specs=pl.BlockSpec((2, 1, 2, hr, tn), lambda j: (0, 0, 0, 0, 0)),
        out_shape=jax.ShapeDtypeStruct((2, 1, 2, hr, tn), jnp.bfloat16),
        compiler_params=pltpu.CompilerParams(vmem_limit_bytes=48 * 1024 * 1024),
    )(tokens, gq, gsr, uq, usr)


def down_kernel(gi, h_ref, q_ref, s_ref, o_ref):
    tk = q_ref.shape[0]
    nb = tk // BLK
    parts = []
    for b in range(nb):
        qb = q_ref[b * BLK:(b + 1) * BLK, :].astype(jnp.float32)
        r = gi * nb + b
        parts.append((qb * s_ref[r:r + 1, :]).astype(jnp.bfloat16))
    w = jnp.concatenate(parts, axis=0)
    o_ref[...] = jnp.dot(h_ref[...], w, preferred_element_type=jnp.float32)


def down(hidden, dq, dsr, gi):
    rows, tk = hidden.shape
    cols = dq.shape[1]
    if not USE_PALLAS:
        w = (dq.astype(jnp.float32) * jnp.repeat(dsr, BLK, axis=0)).astype(jnp.bfloat16)
        return jnp.dot(hidden, w[gi * tk:(gi + 1) * tk], preferred_element_type=jnp.float32)
    return pl.pallas_call(
        functools.partial(down_kernel, gi),
        grid=(1,),
        in_specs=[
            pl.BlockSpec((rows, tk), lambda k: (0, 0)),
            pl.BlockSpec((tk, cols), lambda k: (gi, 0)),
            pl.BlockSpec(dsr.shape, lambda k: (0, 0)),
        ],
        out_specs=pl.BlockSpec((rows, cols), lambda k: (0, 0)),
        out_shape=jax.ShapeDtypeStruct((rows, cols), jnp.float32),
    )(hidden, dq, dsr)


def hid_sum(pout, n_hid):
    pb = pout.astype(jnp.bfloat16)
    from_minus = lax.ppermute(pb, "hid", perm_hid(n_hid, 1))
    from_plus = lax.ppermute(pb, "hid", perm_hid(n_hid, -1))
    hr = pout.shape[0] // 2
    fwd_a = lax.ppermute(from_minus[:hr], "hid", perm_hid(n_hid, 1))
    fwd_b = lax.ppermute(from_plus[hr:], "hid", perm_hid(n_hid, -1))
    far = jnp.concatenate([fwd_a, fwd_b], axis=0).astype(jnp.float32)
    return pout + from_minus.astype(jnp.float32) + from_plus.astype(jnp.float32) + far


def shards(n_hid, tokens, gate_quant, gate_scale, up_quant, up_scale, down_quant, down_scale):
    w = lax.axis_index("wid")
    c = w % NC
    x = (w // NC) % NX
    z = w // (NC * NX)
    rows = tokens.shape[0]
    hr = rows // 2

    tok = jnp.concatenate([tokens, tokens], axis=0)
    tok = lax.dynamic_slice_in_dim(tok, c * hr, rows, 0)
    gsr = jnp.repeat(gate_scale, BLK, axis=1)
    usr = jnp.repeat(up_scale, BLK, axis=1)
    dsr = jnp.repeat(down_scale, BLK, axis=1)

    pc = perm_core()
    p_mine = p_other = None
    for gi in range(GROUPS):
        out = gate_up(tok, gate_quant, gsr, up_quant, usr, gi)
        recv = lax.ppermute(out[1, 0], "wid", pc)
        q = out[0, 0].astype(jnp.float32) + recv.astype(jnp.float32)
        d = 1 if gi % 2 == 0 else -1
        if gi < 2:
            r1 = ring_rs(q, 1, x, perm_x(d), d, NX)
            r2 = direct_rs(r1, 1, z, perm_z, NZ)
        else:
            r1 = ring_rs(q, 1, z, perm_z(d), d, NZ)
            r2 = direct_rs(r1, 1, x, perm_x, NX)
        hg = (jax.nn.silu(r2[0]) * r2[1]).astype(jnp.bfloat16)
        if gi < 2:
            a1 = direct_ag(hg, z, perm_z, NZ)
            a2 = ring_ag(a1, x, perm_x(d), d, NX)
        else:
            a1 = direct_ag(hg, x, perm_x, NX)
            a2 = ring_ag(a1, z, perm_z(d), d, NZ)
        pm = down(a2, down_quant, dsr, gi)
        po = down(lax.ppermute(a2, "wid", pc), down_quant, dsr, gi)
        p_mine = pm if p_mine is None else p_mine + pm
        p_other = po if p_other is None else p_other + po

    s_mine = hid_sum(p_mine, n_hid)
    s_other = hid_sum(p_other, n_hid)
    rolled = jnp.concatenate([s_mine, s_other, s_mine], axis=0).astype(jnp.bfloat16)
    return lax.dynamic_slice_in_dim(rolled, c * hr, rows, 0)


def solution(mesh):
    n_hid = mesh.shape["hid"]
    assert n_hid == 4 and mesh.shape["wid"] == NZ * NX * NC
    return jax.shard_map(
        functools.partial(shards, n_hid),
        mesh=mesh,
        in_specs=(
            P(None, "wid"),
            P("wid", "hid"),
            P("wid", "hid"),
            P("wid", "hid"),
            P("wid", "hid"),
            P("hid", "wid"),
            P("hid", "wid"),
        ),
        out_specs=P(None, "wid"),
        check_vma=False,
    )
```

```python
import functools

import jax
import jax.numpy as jnp
from jax import lax
from jax.experimental import pallas as pl
from jax.experimental.pallas import tpu as pltpu
from jax.sharding import Mesh
from jax.sharding import PartitionSpec as P

BLK = 128
NC = 2
USE_PALLAS = True


def perm_pairs(n, d):
    return [(i, (i + d) % n) for i in range(n)]


def gate_up_kernel(t_ref, gq_ref, gs_ref, uq_ref, us_ref, o_ref):
    t = t_ref[...]
    kb = t_ref.shape[1] // BLK
    half = o_ref.shape[2]
    for gi, (q_ref, s_ref) in enumerate(((gq_ref, gs_ref), (uq_ref, us_ref))):
        parts = []
        for b in range(kb):
            qb = q_ref[b * BLK:(b + 1) * BLK, :].astype(jnp.float32)
            parts.append((qb * s_ref[b:b + 1, :]).astype(jnp.bfloat16))
        w = jnp.concatenate(parts, axis=0)
        res = jnp.dot(t, w, preferred_element_type=jnp.float32).astype(o_ref.dtype)
        for h in range(2):
            o_ref[h, gi] = res[h * half:(h + 1) * half]


def gate_up(tokens, gq, gs, uq, us):
    rows, k = tokens.shape
    cols = gq.shape[1]
    hr = rows // 2
    gsr = jnp.repeat(gs, BLK, axis=1)
    usr = jnp.repeat(us, BLK, axis=1)
    if not USE_PALLAS:
        def deq(q, sr):
            return (q.astype(jnp.float32) * jnp.repeat(sr, BLK, axis=0)).astype(jnp.bfloat16)
        g = jnp.dot(tokens, deq(gq, gsr), preferred_element_type=jnp.float32).astype(jnp.bfloat16)
        u = jnp.dot(tokens, deq(uq, usr), preferred_element_type=jnp.float32).astype(jnp.bfloat16)
        both = jnp.stack([g, u])
        return both.reshape(2, 2, hr, cols).transpose(1, 0, 2, 3)
    tn = 1664
    nb = k // BLK
    return pl.pallas_call(
        gate_up_kernel,
        grid=(cols // tn,),
        in_specs=[
            pl.BlockSpec((rows, k), lambda j: (0, 0)),
            pl.BlockSpec((k, tn), lambda j: (0, j)),
            pl.BlockSpec((nb, tn), lambda j: (0, j)),
            pl.BlockSpec((k, tn), lambda j: (0, j)),
            pl.BlockSpec((nb, tn), lambda j: (0, j)),
        ],
        out_specs=pl.BlockSpec((2, 2, hr, tn), lambda j: (0, 0, 0, j)),
        out_shape=jax.ShapeDtypeStruct((2, 2, hr, cols), jnp.bfloat16),
        compiler_params=pltpu.CompilerParams(vmem_limit_bytes=48 * 1024 * 1024),
    )(tokens, gq, gsr, uq, usr)


def down_kernel(h_ref, q_ref, s_ref, o_ref):
    k = pl.program_id(0)
    tk = q_ref.shape[0]
    nb = tk // BLK

    @pl.when(k == 0)
    def _():
        o_ref[...] = jnp.zeros_like(o_ref)

    parts = []
    for b in range(nb):
        qb = q_ref[b * BLK:(b + 1) * BLK, :].astype(jnp.float32)
        sb = s_ref[pl.ds(k * nb + b, 1), :]
        parts.append((qb * sb).astype(jnp.bfloat16))
    w = jnp.concatenate(parts, axis=0)
    o_ref[...] += jnp.dot(h_ref[...], w, preferred_element_type=jnp.float32)


def down(hidden, dq, dsr):
    rows, kdim = hidden.shape
    cols = dq.shape[1]
    if not USE_PALLAS:
        w = (dq.astype(jnp.float32) * jnp.repeat(dsr, BLK, axis=0)).astype(jnp.bfloat16)
        return jnp.dot(hidden, w, preferred_element_type=jnp.float32)
    tk = 1664
    return pl.pallas_call(
        down_kernel,
        grid=(kdim // tk,),
        in_specs=[
            pl.BlockSpec((rows, tk), lambda k: (0, k)),
            pl.BlockSpec((tk, cols), lambda k: (k, 0)),
            pl.BlockSpec(dsr.shape, lambda k: (0, 0)),
        ],
        out_specs=pl.BlockSpec((rows, cols), lambda k: (0, 0)),
        out_shape=jax.ShapeDtypeStruct((rows, cols), jnp.float32),
    )(hidden, dq, dsr)


def hid_sum(pout, n_hid):
    pb = pout.astype(jnp.bfloat16)
    from_minus = lax.ppermute(pb, "hid", perm_pairs(n_hid, 1))
    from_plus = lax.ppermute(pb, "hid", perm_pairs(n_hid, -1))
    hr = pout.shape[0] // 2
    fwd_a = lax.ppermute(from_minus[:hr], "hid", perm_pairs(n_hid, 1))
    fwd_b = lax.ppermute(from_plus[hr:], "hid", perm_pairs(n_hid, -1))
    far = jnp.concatenate([fwd_a, fwd_b], axis=0).astype(jnp.float32)
    return pout + from_minus.astype(jnp.float32) + from_plus.astype(jnp.float32) + far


def shards(n_hid, n_chip, tokens, gate_quant, gate_scale, up_quant, up_scale, down_quant, down_scale):
    c = lax.axis_index("c")
    rows = tokens.shape[0]
    cols = gate_quant.shape[1]
    hr = rows // 2
    br = hr // n_chip

    tok = jnp.concatenate([tokens, tokens], axis=0)
    tok = lax.dynamic_slice_in_dim(tok, c * hr, rows, 0)
    out = gate_up(tok, gate_quant, gate_scale, up_quant, up_scale)

    pc = perm_pairs(NC, 1)
    recv = lax.ppermute(out[1], "c", pc)
    q = out[0].astype(jnp.float32) + recv.astype(jnp.float32)
    qb = q.astype(jnp.bfloat16).reshape(2, n_chip, br, cols)
    got = lax.all_to_all(qb, "chip", 1, 1)
    r = jnp.sum(got.astype(jnp.float32), axis=1)
    hg = (jax.nn.silu(r[0]) * r[1]).astype(jnp.bfloat16)
    hb = jnp.broadcast_to(hg[None], (n_chip, br, cols))
    hmine = lax.all_to_all(hb, "chip", 0, 0).reshape(hr, cols)
    hother = lax.ppermute(hmine, "c", pc)

    dsr = jnp.repeat(down_scale, BLK, axis=1)
    s_mine = hid_sum(down(hmine, down_quant, dsr), n_hid)
    s_other = hid_sum(down(hother, down_quant, dsr), n_hid)
    rolled = jnp.concatenate([s_mine, s_other, s_mine], axis=0).astype(jnp.bfloat16)
    return lax.dynamic_slice_in_dim(rolled, c * hr, rows, 0)


def solution(mesh):
    n_hid = mesh.shape["hid"]
    n_wid = mesh.shape["wid"]
    n_chip = n_wid // NC
    view = Mesh(mesh.devices.reshape(n_hid, n_chip, NC), ("hid", "chip", "c"))
    wid = ("chip", "c")
    return jax.shard_map(
        functools.partial(shards, n_hid, n_chip),
        mesh=view,
        in_specs=(
            P(None, wid),
            P(wid, "hid"),
            P(wid, "hid"),
            P(wid, "hid"),
            P(wid, "hid"),
            P("hid", wid),
            P("hid", wid),
        ),
        out_specs=P(None, wid),
        check_vma=False,
    )
```

```python
import functools

import jax
import jax.numpy as jnp
from jax import lax
from jax.experimental import pallas as pl
from jax.experimental.pallas import tpu as pltpu
from jax.sharding import PartitionSpec as P

BLK = 128
NZ, NX, NC = 4, 4, 2
GROUPS = 2
TN = 1664
USE_PALLAS = True


def wid_of(z, x, c):
    return (z * NX + x) * NC + c


def perm_core():
    return [(wid_of(z, x, c), wid_of(z, x, 1 - c)) for z in range(NZ) for x in range(NX) for c in range(NC)]


def perm_x(d):
    return [(wid_of(z, x, c), wid_of(z, (x + d) % NX, c)) for z in range(NZ) for x in range(NX) for c in range(NC)]


def perm_z(d):
    return [(wid_of(z, x, c), wid_of((z + d) % NZ, x, c)) for z in range(NZ) for x in range(NX) for c in range(NC)]


def perm_x_split():
    return [(wid_of(z, x, c), wid_of(z, (x + 1 - 2 * c) % NX, c)) for z in range(NZ) for x in range(NX) for c in range(NC)]


def perm_z_split():
    return [(wid_of(z, x, c), wid_of((z + 1 - 2 * c) % NZ, x, c)) for z in range(NZ) for x in range(NX) for c in range(NC)]


def perm_hid(n, d):
    return [(h, (h + d) % n) for h in range(n)]


def ring_rs(arr, axis, pos, perm, d, n):
    size = arr.shape[axis] // n

    def own(j):
        return lax.dynamic_slice_in_dim(arr, j * size, size, axis).astype(jnp.float32)

    send = own((pos - d) % n)
    acc = None
    for s in range(n - 1):
        recv = lax.ppermute(send.astype(jnp.bfloat16), "wid", perm).astype(jnp.float32)
        acc = recv + own((pos - d * (s + 2)) % n)
        send = acc
    return acc


def ring_ag(chunk, pos, perm, d, n):
    rows = chunk.shape[0]
    out = jnp.zeros((n * rows,) + chunk.shape[1:], chunk.dtype)

    def put(o, c, j):
        return lax.dynamic_update_slice_in_dim(o, c, j * rows, 0)

    out = put(out, chunk, pos)
    send = chunk
    for s in range(n - 1):
        recv = lax.ppermute(send, "wid", perm)
        out = put(out, recv, (pos - d * (s + 1)) % n)
        send = recv
    return out


def gate_up_kernel(t_ref, gq_ref, gs_ref, uq_ref, us_ref, o_ref):
    t = t_ref[...]
    kb = t_ref.shape[1] // BLK
    half = o_ref.shape[3]
    for gi, (q_ref, s_ref) in enumerate(((gq_ref, gs_ref), (uq_ref, us_ref))):
        parts = []
        for b in range(kb):
            qb = q_ref[b * BLK:(b + 1) * BLK, :].astype(jnp.float32)
            parts.append((qb * s_ref[b:b + 1, :]).astype(jnp.bfloat16))
        w = jnp.concatenate(parts, axis=0)
        res = jnp.dot(t, w, preferred_element_type=jnp.float32).astype(o_ref.dtype)
        for h in range(2):
            o_ref[h, 0, gi] = res[h * half:(h + 1) * half]


def gate_up(tokens, gq, gs, uq, us):
    rows, k = tokens.shape
    cols = gq.shape[1]
    tn = cols // GROUPS
    hr = rows // 2
    gsr = jnp.repeat(gs, BLK, axis=1)
    usr = jnp.repeat(us, BLK, axis=1)
    if not USE_PALLAS:
        def deq(q, sr):
            return (q.astype(jnp.float32) * jnp.repeat(sr, BLK, axis=0)).astype(jnp.bfloat16)
        g = jnp.dot(tokens, deq(gq, gsr), preferred_element_type=jnp.float32).astype(jnp.bfloat16)
        u = jnp.dot(tokens, deq(uq, usr), preferred_element_type=jnp.float32).astype(jnp.bfloat16)
        both = jnp.stack([g, u])
        both = both.reshape(2, 2, hr, GROUPS, tn)
        return both.transpose(1, 3, 0, 2, 4)
    nb = k // BLK
    sub = tn // TN
    return pl.pallas_call(
        gate_up_kernel,
        grid=(cols // TN,),
        in_specs=[
            pl.BlockSpec((rows, k), lambda j: (0, 0)),
            pl.BlockSpec((k, TN), lambda j: (0, j)),
            pl.BlockSpec((nb, TN), lambda j: (0, j)),
            pl.BlockSpec((k, TN), lambda j: (0, j)),
            pl.BlockSpec((nb, TN), lambda j: (0, j)),
        ],
        out_specs=pl.BlockSpec((2, 1, 2, hr, TN), lambda j: (0, j // sub, 0, 0, j % sub)),
        out_shape=jax.ShapeDtypeStruct((2, GROUPS, 2, hr, tn), jnp.bfloat16),
        compiler_params=pltpu.CompilerParams(vmem_limit_bytes=48 * 1024 * 1024),
    )(tokens, gq, gsr, uq, usr)


def down_kernel(h_ref, q_ref, s_ref, o_ref):
    k = pl.program_id(0)
    tk = q_ref.shape[0]
    nb = tk // BLK

    @pl.when(k == 0)
    def _():
        o_ref[...] = jnp.zeros_like(o_ref)

    parts = []
    for b in range(nb):
        qb = q_ref[b * BLK:(b + 1) * BLK, :].astype(jnp.float32)
        sb = s_ref[pl.ds(k * nb + b, 1), :]
        parts.append((qb * sb).astype(jnp.bfloat16))
    w = jnp.concatenate(parts, axis=0)
    o_ref[...] += jnp.dot(h_ref[0], w, preferred_element_type=jnp.float32)


def down(hidden, dq, dsr):
    groups, rows, tk = hidden.shape
    cols = dq.shape[1]
    if not USE_PALLAS:
        w = (dq.astype(jnp.float32) * jnp.repeat(dsr, BLK, axis=0)).astype(jnp.bfloat16)
        h = hidden.transpose(1, 0, 2).reshape(rows, groups * tk)
        return jnp.dot(h, w, preferred_element_type=jnp.float32)
    sub = tk // TN
    return pl.pallas_call(
        down_kernel,
        grid=(groups * sub,),
        in_specs=[
            pl.BlockSpec((1, rows, TN), lambda k: (k // sub, 0, k % sub)),
            pl.BlockSpec((TN, cols), lambda k: (k, 0)),
            pl.BlockSpec(dsr.shape, lambda k: (0, 0)),
        ],
        out_specs=pl.BlockSpec((rows, cols), lambda k: (0, 0)),
        out_shape=jax.ShapeDtypeStruct((rows, cols), jnp.float32),
    )(hidden, dq, dsr)


def hid_sum(pout, n_hid):
    pb = pout.astype(jnp.bfloat16)
    from_minus = lax.ppermute(pb, "hid", perm_hid(n_hid, 1))
    from_plus = lax.ppermute(pb, "hid", perm_hid(n_hid, -1))
    hr = pout.shape[0] // 2
    fwd_a = lax.ppermute(from_minus[:hr], "hid", perm_hid(n_hid, 1))
    fwd_b = lax.ppermute(from_plus[hr:], "hid", perm_hid(n_hid, -1))
    far = jnp.concatenate([fwd_a, fwd_b], axis=0).astype(jnp.float32)
    return pout + from_minus.astype(jnp.float32) + from_plus.astype(jnp.float32) + far


def shards(n_hid, tokens, gate_quant, gate_scale, up_quant, up_scale, down_quant, down_scale):
    w = lax.axis_index("wid")
    c = w % NC
    x = (w // NC) % NX
    z = w // (NC * NX)
    rows = tokens.shape[0]
    hr = rows // 2

    tok = jnp.concatenate([tokens, tokens], axis=0)
    tok = lax.dynamic_slice_in_dim(tok, c * hr, rows, 0)
    out = gate_up(tok, gate_quant, gate_scale, up_quant, up_scale)

    pc = perm_core()
    d = 1 - 2 * c
    px, pz = perm_x_split(), perm_z_split()
    hmine, hother = [], []
    for gi in range(GROUPS):
        recv = lax.ppermute(out[1, gi], "wid", pc)
        q = out[0, gi].astype(jnp.float32) + recv.astype(jnp.float32)
        if gi == 0:
            r1 = ring_rs(q, 1, x, px, d, NX)
            r2 = ring_rs(r1, 1, z, pz, d, NZ)
        else:
            r1 = ring_rs(q, 1, z, pz, d, NZ)
            r2 = ring_rs(r1, 1, x, px, d, NX)
        hg = (jax.nn.silu(r2[0]) * r2[1]).astype(jnp.bfloat16)
        if gi == 0:
            a1 = ring_ag(hg, z, pz, d, NZ)
            a2 = ring_ag(a1, x, px, d, NX)
        else:
            a1 = ring_ag(hg, x, px, d, NX)
            a2 = ring_ag(a1, z, pz, d, NZ)
        hmine.append(a2)
        hother.append(lax.ppermute(a2, "wid", pc))

    dsr = jnp.repeat(down_scale, BLK, axis=1)
    p_mine = down(jnp.stack(hmine), down_quant, dsr)
    s_mine = hid_sum(p_mine, n_hid)
    p_other = down(jnp.stack(hother), down_quant, dsr)
    s_other = hid_sum(p_other, n_hid)
    rolled = jnp.concatenate([s_mine, s_other, s_mine], axis=0).astype(jnp.bfloat16)
    return lax.dynamic_slice_in_dim(rolled, c * hr, rows, 0)


def solution(mesh):
    n_hid = mesh.shape["hid"]
    assert n_hid == 4 and mesh.shape["wid"] == NZ * NX * NC
    return jax.shard_map(
        functools.partial(shards, n_hid),
        mesh=mesh,
        in_specs=(
            P(None, "wid"),
            P("wid", "hid"),
            P("wid", "hid"),
            P("wid", "hid"),
            P("wid", "hid"),
            P("hid", "wid"),
            P("hid", "wid"),
        ),
        out_specs=P(None, "wid"),
        check_vma=False,
    )
```

```python
import functools

import jax
import jax.numpy as jnp
from jax import lax
from jax.experimental import pallas as pl
from jax.experimental.pallas import tpu as pltpu
from jax.sharding import PartitionSpec as P

BLK = 128
NZ, NX, NC = 4, 4, 2
GROUPS = 4
USE_PALLAS = True


def wid_of(z, x, c):
    return (z * NX + x) * NC + c


def perm_core():
    return [(wid_of(z, x, c), wid_of(z, x, 1 - c)) for z in range(NZ) for x in range(NX) for c in range(NC)]


def perm_x(d):
    return [(wid_of(z, x, c), wid_of(z, (x + d) % NX, c)) for z in range(NZ) for x in range(NX) for c in range(NC)]


def perm_z(d):
    return [(wid_of(z, x, c), wid_of((z + d) % NZ, x, c)) for z in range(NZ) for x in range(NX) for c in range(NC)]


def perm_hid(n, d):
    return [(h, (h + d) % n) for h in range(n)]


def ring_rs(arr, axis, pos, perm, d, n):
    size = arr.shape[axis] // n

    def own(j):
        return lax.dynamic_slice_in_dim(arr, j * size, size, axis).astype(jnp.float32)

    send = own((pos - d) % n)
    acc = None
    for s in range(n - 1):
        recv = lax.ppermute(send.astype(jnp.bfloat16), "wid", perm).astype(jnp.float32)
        acc = recv + own((pos - d * (s + 2)) % n)
        send = acc
    return acc


def ring_ag(chunk, pos, perm, d, n, buf=None, slot=0):
    rows = chunk.shape[0]
    if buf is None:
        out = jnp.zeros((n * rows,) + chunk.shape[1:], chunk.dtype)

        def put(o, c, j):
            return lax.dynamic_update_slice_in_dim(o, c, j * rows, 0)
    else:
        out = buf

        def put(o, c, j):
            return lax.dynamic_update_slice(o, c[None], (slot, j * rows, 0))

    out = put(out, chunk, pos)
    send = chunk
    for s in range(n - 1):
        recv = lax.ppermute(send, "wid", perm)
        out = put(out, recv, (pos - d * (s + 1)) % n)
        send = recv
    return out


def gate_up_kernel(t_ref, gq_ref, gs_ref, uq_ref, us_ref, o_ref):
    t = t_ref[...]
    kb = t_ref.shape[1] // BLK
    half = o_ref.shape[3]
    for gi, (q_ref, s_ref) in enumerate(((gq_ref, gs_ref), (uq_ref, us_ref))):
        parts = []
        for b in range(kb):
            qb = q_ref[b * BLK:(b + 1) * BLK, :].astype(jnp.float32)
            parts.append((qb * s_ref[b:b + 1, :]).astype(jnp.bfloat16))
        w = jnp.concatenate(parts, axis=0)
        res = jnp.dot(t, w, preferred_element_type=jnp.float32).astype(o_ref.dtype)
        for h in range(2):
            o_ref[h, 0, gi] = res[h * half:(h + 1) * half]


def gate_up(tokens, gq, gs, uq, us):
    rows, k = tokens.shape
    cols = gq.shape[1]
    tn = cols // GROUPS
    hr = rows // 2
    gsr = jnp.repeat(gs, BLK, axis=1)
    usr = jnp.repeat(us, BLK, axis=1)
    if not USE_PALLAS:
        def deq(q, sr):
            return (q.astype(jnp.float32) * jnp.repeat(sr, BLK, axis=0)).astype(jnp.bfloat16)
        g = jnp.dot(tokens, deq(gq, gsr), preferred_element_type=jnp.float32).astype(jnp.bfloat16)
        u = jnp.dot(tokens, deq(uq, usr), preferred_element_type=jnp.float32).astype(jnp.bfloat16)
        both = jnp.stack([g, u])
        both = both.reshape(2, 2, hr, GROUPS, tn)
        return both.transpose(1, 3, 0, 2, 4)
    nb = k // BLK
    return pl.pallas_call(
        gate_up_kernel,
        grid=(GROUPS,),
        in_specs=[
            pl.BlockSpec((rows, k), lambda j: (0, 0)),
            pl.BlockSpec((k, tn), lambda j: (0, j)),
            pl.BlockSpec((nb, tn), lambda j: (0, j)),
            pl.BlockSpec((k, tn), lambda j: (0, j)),
            pl.BlockSpec((nb, tn), lambda j: (0, j)),
        ],
        out_specs=pl.BlockSpec((2, 1, 2, hr, tn), lambda j: (0, j, 0, 0, 0)),
        out_shape=jax.ShapeDtypeStruct((2, GROUPS, 2, hr, tn), jnp.bfloat16),
        compiler_params=pltpu.CompilerParams(vmem_limit_bytes=48 * 1024 * 1024),
    )(tokens, gq, gsr, uq, usr)


def down_kernel(h_ref, q_ref, s_ref, o_ref):
    k = pl.program_id(0)
    tk = q_ref.shape[0]
    nb = tk // BLK

    @pl.when(k == 0)
    def _():
        o_ref[...] = jnp.zeros_like(o_ref)

    parts = []
    for b in range(nb):
        qb = q_ref[b * BLK:(b + 1) * BLK, :].astype(jnp.float32)
        sb = s_ref[pl.ds(k * nb + b, 1), :]
        parts.append((qb * sb).astype(jnp.bfloat16))
    w = jnp.concatenate(parts, axis=0)
    o_ref[...] += jnp.dot(h_ref[0], w, preferred_element_type=jnp.float32)


def down(hidden, dq, dsr):
    groups, rows, tk = hidden.shape
    cols = dq.shape[1]
    if not USE_PALLAS:
        w = (dq.astype(jnp.float32) * jnp.repeat(dsr, BLK, axis=0)).astype(jnp.bfloat16)
        h = hidden.transpose(1, 0, 2).reshape(rows, groups * tk)
        return jnp.dot(h, w, preferred_element_type=jnp.float32)
    return pl.pallas_call(
        down_kernel,
        grid=(groups,),
        in_specs=[
            pl.BlockSpec((1, rows, tk), lambda k: (k, 0, 0)),
            pl.BlockSpec((tk, cols), lambda k: (k, 0)),
            pl.BlockSpec(dsr.shape, lambda k: (0, 0)),
        ],
        out_specs=pl.BlockSpec((rows, cols), lambda k: (0, 0)),
        out_shape=jax.ShapeDtypeStruct((rows, cols), jnp.float32),
    )(hidden, dq, dsr)


def hid_sum(pout, n_hid):
    pb = pout.astype(jnp.bfloat16)
    from_minus = lax.ppermute(pb, "hid", perm_hid(n_hid, 1))
    from_plus = lax.ppermute(pb, "hid", perm_hid(n_hid, -1))
    hr = pout.shape[0] // 2
    fwd_a = lax.ppermute(from_minus[:hr], "hid", perm_hid(n_hid, 1))
    fwd_b = lax.ppermute(from_plus[hr:], "hid", perm_hid(n_hid, -1))
    far = jnp.concatenate([fwd_a, fwd_b], axis=0).astype(jnp.float32)
    return pout + from_minus.astype(jnp.float32) + from_plus.astype(jnp.float32) + far


def shards(n_hid, tokens, gate_quant, gate_scale, up_quant, up_scale, down_quant, down_scale):
    w = lax.axis_index("wid")
    c = w % NC
    x = (w // NC) % NX
    z = w // (NC * NX)
    rows = tokens.shape[0]
    hr = rows // 2

    tok = jnp.concatenate([tokens, tokens], axis=0)
    tok = lax.dynamic_slice_in_dim(tok, c * hr, rows, 0)
    out = gate_up(tok, gate_quant, gate_scale, up_quant, up_scale)

    pc = perm_core()
    tn = out.shape[-1]
    hmine = jnp.zeros((GROUPS, hr, tn), jnp.bfloat16)
    hother = jnp.zeros((GROUPS, hr, tn), jnp.bfloat16)
    for gi in range(GROUPS):
        recv = lax.ppermute(out[1, gi], "wid", pc)
        q = (out[0, gi].astype(jnp.float32) + recv.astype(jnp.float32)).astype(jnp.bfloat16)
        d = 1 if gi % 2 == 0 else -1
        if gi < 2:
            r1 = ring_rs(q, 1, x, perm_x(d), d, NX)
            r2 = ring_rs(r1, 1, z, perm_z(d), d, NZ)
        else:
            r1 = ring_rs(q, 1, z, perm_z(d), d, NZ)
            r2 = ring_rs(r1, 1, x, perm_x(d), d, NX)
        hg = (jax.nn.silu(r2[0]) * r2[1]).astype(jnp.bfloat16)
        if gi < 2:
            a1 = ring_ag(hg, z, perm_z(d), d, NZ)
            hmine = ring_ag(a1, x, perm_x(d), d, NX, hmine, gi)
        else:
            a1 = ring_ag(hg, x, perm_x(d), d, NX)
            hmine = ring_ag(a1, z, perm_z(d), d, NZ, hmine, gi)
        hother = lax.dynamic_update_slice(hother, lax.ppermute(hmine[gi], "wid", pc)[None], (gi, 0, 0))

    dsr = jnp.repeat(down_scale, BLK, axis=1)
    p_mine = down(hmine, down_quant, dsr)
    s_mine = hid_sum(p_mine, n_hid)
    p_other = down(hother, down_quant, dsr)
    s_other = hid_sum(p_other, n_hid)
    rolled = jnp.concatenate([s_mine, s_other, s_mine], axis=0).astype(jnp.bfloat16)
    return lax.dynamic_slice_in_dim(rolled, c * hr, rows, 0)


def solution(mesh):
    n_hid = mesh.shape["hid"]
    assert n_hid == 4 and mesh.shape["wid"] == NZ * NX * NC
    return jax.shard_map(
        functools.partial(shards, n_hid),
        mesh=mesh,
        in_specs=(
            P(None, "wid"),
            P("wid", "hid"),
            P("wid", "hid"),
            P("wid", "hid"),
            P("wid", "hid"),
            P("hid", "wid"),
            P("hid", "wid"),
        ),
        out_specs=P(None, "wid"),
        check_vma=False,
    )
```

```python
import functools

import jax
import jax.numpy as jnp
from jax import lax
from jax.experimental import pallas as pl
from jax.experimental.pallas import tpu as pltpu
from jax.sharding import Mesh
from jax.sharding import PartitionSpec as P

BLK = 128
NZ, NX, NC = 4, 4, 2
WID = ("chip", "c")
GROUPS = 4
USE_PALLAS = True


def wid_of(z, x, c):
    return (z * NX + x) * NC + c


def perm_core():
    return [(wid_of(z, x, c), wid_of(z, x, 1 - c)) for z in range(NZ) for x in range(NX) for c in range(NC)]


def perm_x(d):
    return [(wid_of(z, x, c), wid_of(z, (x + d) % NX, c)) for z in range(NZ) for x in range(NX) for c in range(NC)]


def perm_z(d):
    return [(wid_of(z, x, c), wid_of((z + d) % NZ, x, c)) for z in range(NZ) for x in range(NX) for c in range(NC)]


def perm_hid(n, d):
    return [(h, (h + d) % n) for h in range(n)]


def ring_rs(arr, axis, pos, perm, d, n):
    size = arr.shape[axis] // n

    def own(j):
        return lax.dynamic_slice_in_dim(arr, j * size, size, axis).astype(jnp.float32)

    send = own((pos - d) % n)
    acc = None
    for s in range(n - 1):
        recv = lax.ppermute(send.astype(jnp.bfloat16), WID, perm).astype(jnp.float32)
        acc = recv + own((pos - d * (s + 2)) % n)
        send = acc
    return acc


def ring_ag(chunk, pos, perm, d, n):
    rows = chunk.shape[0]
    out = jnp.zeros((n * rows,) + chunk.shape[1:], chunk.dtype)

    def put(o, c, j):
        return lax.dynamic_update_slice_in_dim(o, c, j * rows, 0)

    out = put(out, chunk, pos)
    send = chunk
    for s in range(n - 1):
        recv = lax.ppermute(send, WID, perm)
        out = put(out, recv, (pos - d * (s + 1)) % n)
        send = recv
    return out


def gate_up_kernel(t_ref, gq_ref, gs_ref, uq_ref, us_ref, o_ref):
    t = t_ref[...]
    kb = t_ref.shape[1] // BLK
    half = o_ref.shape[3]
    for gi, (q_ref, s_ref) in enumerate(((gq_ref, gs_ref), (uq_ref, us_ref))):
        parts = []
        for b in range(kb):
            qb = q_ref[b * BLK:(b + 1) * BLK, :].astype(jnp.float32)
            parts.append((qb * s_ref[b:b + 1, :]).astype(jnp.bfloat16))
        w = jnp.concatenate(parts, axis=0)
        res = jnp.dot(t, w, preferred_element_type=jnp.float32).astype(o_ref.dtype)
        for h in range(2):
            o_ref[h, 0, gi] = res[h * half:(h + 1) * half]


def gate_up(tokens, gq, gs, uq, us):
    rows, k = tokens.shape
    cols = gq.shape[1]
    tn = cols // GROUPS
    hr = rows // 2
    gsr = jnp.repeat(gs, BLK, axis=1)
    usr = jnp.repeat(us, BLK, axis=1)
    if not USE_PALLAS:
        def deq(q, sr):
            return (q.astype(jnp.float32) * jnp.repeat(sr, BLK, axis=0)).astype(jnp.bfloat16)
        g = jnp.dot(tokens, deq(gq, gsr), preferred_element_type=jnp.float32).astype(jnp.bfloat16)
        u = jnp.dot(tokens, deq(uq, usr), preferred_element_type=jnp.float32).astype(jnp.bfloat16)
        both = jnp.stack([g, u])
        both = both.reshape(2, 2, hr, GROUPS, tn)
        return both.transpose(1, 3, 0, 2, 4)
    nb = k // BLK
    return pl.pallas_call(
        gate_up_kernel,
        grid=(GROUPS,),
        in_specs=[
            pl.BlockSpec((rows, k), lambda j: (0, 0)),
            pl.BlockSpec((k, tn), lambda j: (0, j)),
            pl.BlockSpec((nb, tn), lambda j: (0, j)),
            pl.BlockSpec((k, tn), lambda j: (0, j)),
            pl.BlockSpec((nb, tn), lambda j: (0, j)),
        ],
        out_specs=pl.BlockSpec((2, 1, 2, hr, tn), lambda j: (0, j, 0, 0, 0)),
        out_shape=jax.ShapeDtypeStruct((2, GROUPS, 2, hr, tn), jnp.bfloat16),
        compiler_params=pltpu.CompilerParams(vmem_limit_bytes=48 * 1024 * 1024),
    )(tokens, gq, gsr, uq, usr)


def down_kernel(h_ref, q_ref, s_ref, o_ref):
    k = pl.program_id(0)
    tk = q_ref.shape[0]
    nb = tk // BLK

    @pl.when(k == 0)
    def _():
        o_ref[...] = jnp.zeros_like(o_ref)

    parts = []
    for b in range(nb):
        qb = q_ref[b * BLK:(b + 1) * BLK, :].astype(jnp.float32)
        sb = s_ref[pl.ds(k * nb + b, 1), :]
        parts.append((qb * sb).astype(jnp.bfloat16))
    w = jnp.concatenate(parts, axis=0)
    o_ref[...] += jnp.dot(h_ref[0], w, preferred_element_type=jnp.float32)


def down(hidden, dq, dsr):
    groups, rows, tk = hidden.shape
    cols = dq.shape[1]
    if not USE_PALLAS:
        w = (dq.astype(jnp.float32) * jnp.repeat(dsr, BLK, axis=0)).astype(jnp.bfloat16)
        h = hidden.transpose(1, 0, 2).reshape(rows, groups * tk)
        return jnp.dot(h, w, preferred_element_type=jnp.float32)
    return pl.pallas_call(
        down_kernel,
        grid=(groups,),
        in_specs=[
            pl.BlockSpec((1, rows, tk), lambda k: (k, 0, 0)),
            pl.BlockSpec((tk, cols), lambda k: (k, 0)),
            pl.BlockSpec(dsr.shape, lambda k: (0, 0)),
        ],
        out_specs=pl.BlockSpec((rows, cols), lambda k: (0, 0)),
        out_shape=jax.ShapeDtypeStruct((rows, cols), jnp.float32),
    )(hidden, dq, dsr)


def hid_sum(pout, n_hid):
    pb = pout.astype(jnp.bfloat16)
    from_minus = lax.ppermute(pb, "hid", perm_hid(n_hid, 1))
    from_plus = lax.ppermute(pb, "hid", perm_hid(n_hid, -1))
    hr = pout.shape[0] // 2
    fwd_a = lax.ppermute(from_minus[:hr], "hid", perm_hid(n_hid, 1))
    fwd_b = lax.ppermute(from_plus[hr:], "hid", perm_hid(n_hid, -1))
    far = jnp.concatenate([fwd_a, fwd_b], axis=0).astype(jnp.float32)
    return pout + from_minus.astype(jnp.float32) + from_plus.astype(jnp.float32) + far


def shards(n_hid, tokens, gate_quant, gate_scale, up_quant, up_scale, down_quant, down_scale):
    chip = lax.axis_index("chip")
    c = lax.axis_index("c")
    x = chip % NX
    z = chip // NX
    rows = tokens.shape[0]
    hr = rows // 2

    tok = jnp.concatenate([tokens, tokens], axis=0)
    tok = lax.dynamic_slice_in_dim(tok, c * hr, rows, 0)
    out = gate_up(tok, gate_quant, gate_scale, up_quant, up_scale)

    pc = perm_core()
    hmine, hother = [], []
    for gi in range(GROUPS):
        recv = lax.ppermute(out[1, gi], WID, pc)
        q = out[0, gi].astype(jnp.float32) + recv.astype(jnp.float32)
        d = 1 if gi % 2 == 0 else -1
        if gi == GROUPS - 1:
            r2 = lax.psum_scatter(q.astype(jnp.bfloat16), "chip", scatter_dimension=1, tiled=True)
            r2 = r2.astype(jnp.float32)
        elif gi < 2:
            r1 = ring_rs(q, 1, x, perm_x(d), d, NX)
            r2 = ring_rs(r1, 1, z, perm_z(d), d, NZ)
        else:
            r1 = ring_rs(q, 1, z, perm_z(d), d, NZ)
            r2 = ring_rs(r1, 1, x, perm_x(d), d, NX)
        hg = (jax.nn.silu(r2[0]) * r2[1]).astype(jnp.bfloat16)
        if gi == GROUPS - 1:
            a2 = lax.all_gather(hg, "chip", axis=0, tiled=True)
        elif gi < 2:
            a1 = ring_ag(hg, z, perm_z(d), d, NZ)
            a2 = ring_ag(a1, x, perm_x(d), d, NX)
        else:
            a1 = ring_ag(hg, x, perm_x(d), d, NX)
            a2 = ring_ag(a1, z, perm_z(d), d, NZ)
        hmine.append(a2)
        hother.append(lax.ppermute(a2, WID, pc))

    dsr = jnp.repeat(down_scale, BLK, axis=1)
    p_mine = down(jnp.stack(hmine), down_quant, dsr)
    s_mine = hid_sum(p_mine, n_hid)
    p_other = down(jnp.stack(hother), down_quant, dsr)
    s_other = hid_sum(p_other, n_hid)
    rolled = jnp.concatenate([s_mine, s_other, s_mine], axis=0).astype(jnp.bfloat16)
    return lax.dynamic_slice_in_dim(rolled, c * hr, rows, 0)


def solution(mesh):
    n_hid = mesh.shape["hid"]
    assert n_hid == 4 and mesh.shape["wid"] == NZ * NX * NC
    view = Mesh(mesh.devices.reshape(n_hid, NZ * NX, NC), ("hid",) + WID)
    return jax.shard_map(
        functools.partial(shards, n_hid),
        mesh=view,
        in_specs=(
            P(None, WID),
            P(WID, "hid"),
            P(WID, "hid"),
            P(WID, "hid"),
            P(WID, "hid"),
            P("hid", WID),
            P("hid", WID),
        ),
        out_specs=P(None, WID),
        check_vma=False,
    )
```

```python
import functools

import jax
import jax.numpy as jnp
from jax import lax
from jax.experimental import pallas as pl
from jax.experimental.pallas import tpu as pltpu
from jax.sharding import PartitionSpec as P

BLK = 128
NZ, NX, NC = 4, 4, 2
GROUPS = 4
USE_PALLAS = True


def wid_of(z, x, c):
    return (z * NX + x) * NC + c


def perm_core():
    return [(wid_of(z, x, c), wid_of(z, x, 1 - c)) for z in range(NZ) for x in range(NX) for c in range(NC)]


def perm_x(d):
    return [(wid_of(z, x, c), wid_of(z, (x + d) % NX, c)) for z in range(NZ) for x in range(NX) for c in range(NC)]


def perm_z(d):
    return [(wid_of(z, x, c), wid_of((z + d) % NZ, x, c)) for z in range(NZ) for x in range(NX) for c in range(NC)]


def perm_hid(n, d):
    return [(h, (h + d) % n) for h in range(n)]


def ring_rs(arr, axis, pos, perm, d, n):
    size = arr.shape[axis] // n

    def own(j):
        return lax.dynamic_slice_in_dim(arr, j * size, size, axis).astype(jnp.float32)

    send = own((pos - d) % n)
    acc = None
    for s in range(n - 1):
        recv = lax.ppermute(send.astype(jnp.bfloat16), "wid", perm).astype(jnp.float32)
        acc = recv + own((pos - d * (s + 2)) % n)
        send = acc
    return acc


def ring_ag(chunk, pos, perm, d, n):
    rows = chunk.shape[0]
    out = jnp.zeros((n * rows,) + chunk.shape[1:], chunk.dtype)

    def put(o, c, j):
        return lax.dynamic_update_slice_in_dim(o, c, j * rows, 0)

    out = put(out, chunk, pos)
    send = chunk
    for s in range(n - 1):
        recv = lax.ppermute(send, "wid", perm)
        out = put(out, recv, (pos - d * (s + 1)) % n)
        send = recv
    return out


def gate_up_kernel(t_ref, gq_ref, gs_ref, uq_ref, us_ref, mine_ref, *other_refs):
    j = pl.program_id(0)
    t = t_ref[...]
    kb = t_ref.shape[1] // BLK
    half = mine_ref.shape[2]
    for gi, (q_ref, s_ref) in enumerate(((gq_ref, gs_ref), (uq_ref, us_ref))):
        parts = []
        for b in range(kb):
            qb = q_ref[b * BLK:(b + 1) * BLK, :].astype(jnp.float32)
            parts.append((qb * s_ref[b:b + 1, :]).astype(jnp.bfloat16))
        w = jnp.concatenate(parts, axis=0)
        res = jnp.dot(t, w, preferred_element_type=jnp.float32).astype(mine_ref.dtype)
        mine_ref[0, gi] = res[:half]
        for g, o_ref in enumerate(other_refs):
            @pl.when(j == g)
            def _():
                o_ref[gi] = res[half:]


def gate_up(tokens, gq, gs, uq, us):
    rows, k = tokens.shape
    cols = gq.shape[1]
    tn = cols // GROUPS
    hr = rows // 2
    gsr = jnp.repeat(gs, BLK, axis=1)
    usr = jnp.repeat(us, BLK, axis=1)
    if not USE_PALLAS:
        def deq(q, sr):
            return (q.astype(jnp.float32) * jnp.repeat(sr, BLK, axis=0)).astype(jnp.bfloat16)
        g = jnp.dot(tokens, deq(gq, gsr), preferred_element_type=jnp.float32).astype(jnp.bfloat16)
        u = jnp.dot(tokens, deq(uq, usr), preferred_element_type=jnp.float32).astype(jnp.bfloat16)
        both = jnp.stack([g, u])
        both = both.reshape(2, 2, hr, GROUPS, tn).transpose(1, 3, 0, 2, 4)
        return [both[0]] + [both[1, g] for g in range(GROUPS)]
    nb = k // BLK
    return pl.pallas_call(
        gate_up_kernel,
        grid=(GROUPS,),
        in_specs=[
            pl.BlockSpec((rows, k), lambda j: (0, 0)),
            pl.BlockSpec((k, tn), lambda j: (0, j)),
            pl.BlockSpec((nb, tn), lambda j: (0, j)),
            pl.BlockSpec((k, tn), lambda j: (0, j)),
            pl.BlockSpec((nb, tn), lambda j: (0, j)),
        ],
        out_specs=[pl.BlockSpec((1, 2, hr, tn), lambda j: (j, 0, 0, 0))]
        + [pl.BlockSpec((2, hr, tn), lambda j: (0, 0, 0))] * GROUPS,
        out_shape=[jax.ShapeDtypeStruct((GROUPS, 2, hr, tn), jnp.bfloat16)]
        + [jax.ShapeDtypeStruct((2, hr, tn), jnp.bfloat16)] * GROUPS,
        compiler_params=pltpu.CompilerParams(vmem_limit_bytes=48 * 1024 * 1024),
    )(tokens, gq, gsr, uq, usr)


def down_kernel(h_ref, q_ref, s_ref, o_ref):
    k = pl.program_id(0)
    tk = q_ref.shape[0]
    nb = tk // BLK

    @pl.when(k == 0)
    def _():
        o_ref[...] = jnp.zeros_like(o_ref)

    parts = []
    for b in range(nb):
        qb = q_ref[b * BLK:(b + 1) * BLK, :].astype(jnp.float32)
        sb = s_ref[pl.ds(k * nb + b, 1), :]
        parts.append((qb * sb).astype(jnp.bfloat16))
    w = jnp.concatenate(parts, axis=0)
    o_ref[...] += jnp.dot(h_ref[0], w, preferred_element_type=jnp.float32)


def down(hidden, dq, dsr):
    groups, rows, tk = hidden.shape
    cols = dq.shape[1]
    if not USE_PALLAS:
        w = (dq.astype(jnp.float32) * jnp.repeat(dsr, BLK, axis=0)).astype(jnp.bfloat16)
        h = hidden.transpose(1, 0, 2).reshape(rows, groups * tk)
        return jnp.dot(h, w, preferred_element_type=jnp.float32)
    return pl.pallas_call(
        down_kernel,
        grid=(groups,),
        in_specs=[
            pl.BlockSpec((1, rows, tk), lambda k: (k, 0, 0)),
            pl.BlockSpec((tk, cols), lambda k: (k, 0)),
            pl.BlockSpec(dsr.shape, lambda k: (0, 0)),
        ],
        out_specs=pl.BlockSpec((rows, cols), lambda k: (0, 0)),
        out_shape=jax.ShapeDtypeStruct((rows, cols), jnp.float32),
    )(hidden, dq, dsr)


def hid_sum(pout, n_hid):
    pb = pout.astype(jnp.bfloat16)
    from_minus = lax.ppermute(pb, "hid", perm_hid(n_hid, 1))
    from_plus = lax.ppermute(pb, "hid", perm_hid(n_hid, -1))
    hr = pout.shape[0] // 2
    fwd_a = lax.ppermute(from_minus[:hr], "hid", perm_hid(n_hid, 1))
    fwd_b = lax.ppermute(from_plus[hr:], "hid", perm_hid(n_hid, -1))
    far = jnp.concatenate([fwd_a, fwd_b], axis=0).astype(jnp.float32)
    return pout + from_minus.astype(jnp.float32) + from_plus.astype(jnp.float32) + far


def shards(n_hid, tokens, gate_quant, gate_scale, up_quant, up_scale, down_quant, down_scale):
    w = lax.axis_index("wid")
    c = w % NC
    x = (w // NC) % NX
    z = w // (NC * NX)
    rows = tokens.shape[0]
    hr = rows // 2

    tok = jnp.concatenate([tokens, tokens], axis=0)
    tok = lax.dynamic_slice_in_dim(tok, c * hr, rows, 0)
    mine, *others = gate_up(tok, gate_quant, gate_scale, up_quant, up_scale)

    pc = perm_core()
    hmine, hother = [], []
    for gi in range(GROUPS):
        recv = lax.ppermute(others[gi], "wid", pc)
        q = mine[gi].astype(jnp.float32) + recv.astype(jnp.float32)
        d = 1 if gi % 2 == 0 else -1
        if gi < 2:
            r1 = ring_rs(q, 1, x, perm_x(d), d, NX)
            r2 = ring_rs(r1, 1, z, perm_z(d), d, NZ)
        else:
            r1 = ring_rs(q, 1, z, perm_z(d), d, NZ)
            r2 = ring_rs(r1, 1, x, perm_x(d), d, NX)
        hg = (jax.nn.silu(r2[0]) * r2[1]).astype(jnp.bfloat16)
        if gi < 2:
            a1 = ring_ag(hg, z, perm_z(d), d, NZ)
            a2 = ring_ag(a1, x, perm_x(d), d, NX)
        else:
            a1 = ring_ag(hg, x, perm_x(d), d, NX)
            a2 = ring_ag(a1, z, perm_z(d), d, NZ)
        hmine.append(a2)
        hother.append(lax.ppermute(a2, "wid", pc))

    dsr = jnp.repeat(down_scale, BLK, axis=1)
    p_mine = down(jnp.stack(hmine), down_quant, dsr)
    s_mine = hid_sum(p_mine, n_hid)
    p_other = down(jnp.stack(hother), down_quant, dsr)
    s_other = hid_sum(p_other, n_hid)
    rolled = jnp.concatenate([s_mine, s_other, s_mine], axis=0).astype(jnp.bfloat16)
    return lax.dynamic_slice_in_dim(rolled, c * hr, rows, 0)


def solution(mesh):
    n_hid = mesh.shape["hid"]
    assert n_hid == 4 and mesh.shape["wid"] == NZ * NX * NC
    return jax.shard_map(
        functools.partial(shards, n_hid),
        mesh=mesh,
        in_specs=(
            P(None, "wid"),
            P("wid", "hid"),
            P("wid", "hid"),
            P("wid", "hid"),
            P("wid", "hid"),
            P("hid", "wid"),
            P("hid", "wid"),
        ),
        out_specs=P(None, "wid"),
        check_vma=False,
    )
```

```python
import functools

import jax
import jax.numpy as jnp
from jax import lax
from jax.experimental import pallas as pl
from jax.experimental.pallas import tpu as pltpu
from jax.sharding import PartitionSpec as P

BLK = 128
NZ, NX, NC = 4, 4, 2
GROUPS = 4
USE_PALLAS = True


def wid_of(z, x, c):
    return (z * NX + x) * NC + c


def perm_core():
    return [(wid_of(z, x, c), wid_of(z, x, 1 - c)) for z in range(NZ) for x in range(NX) for c in range(NC)]


def perm_x(d):
    return [(wid_of(z, x, c), wid_of(z, (x + d) % NX, c)) for z in range(NZ) for x in range(NX) for c in range(NC)]


def perm_z(d):
    return [(wid_of(z, x, c), wid_of((z + d) % NZ, x, c)) for z in range(NZ) for x in range(NX) for c in range(NC)]


def perm_hid(n, d):
    return [(h, (h + d) % n) for h in range(n)]


def ring_rs(arr, axis, pos, perm, d, n):
    size = arr.shape[axis] // n

    def own(j):
        return lax.dynamic_slice_in_dim(arr, j * size, size, axis).astype(jnp.float32)

    send = own((pos - d) % n)
    acc = None
    for s in range(n - 1):
        recv = lax.ppermute(send.astype(jnp.bfloat16), "wid", perm).astype(jnp.float32)
        acc = recv + own((pos - d * (s + 2)) % n)
        send = acc
    return acc


def ring_ag(chunk, pos, perm, d, n):
    rows = chunk.shape[0]
    out = jnp.zeros((n * rows,) + chunk.shape[1:], chunk.dtype)

    def put(o, c, j):
        return lax.dynamic_update_slice_in_dim(o, c, j * rows, 0)

    out = put(out, chunk, pos)
    send = chunk
    for s in range(n - 1):
        recv = lax.ppermute(send, "wid", perm)
        out = put(out, recv, (pos - d * (s + 1)) % n)
        send = recv
    return out


def gate_up_kernel(t_ref, gq_ref, gs_ref, uq_ref, us_ref, mine_ref, *other_refs):
    j = pl.program_id(0)
    t = t_ref[...]
    kb = t_ref.shape[1] // BLK
    half = mine_ref.shape[2]
    for gi, (q_ref, s_ref) in enumerate(((gq_ref, gs_ref), (uq_ref, us_ref))):
        parts = []
        for b in range(kb):
            qb = q_ref[b * BLK:(b + 1) * BLK, :].astype(jnp.float32)
            parts.append((qb * s_ref[b:b + 1, :]).astype(jnp.bfloat16))
        w = jnp.concatenate(parts, axis=0)
        res = jnp.dot(t, w, preferred_element_type=jnp.float32).astype(mine_ref.dtype)
        mine_ref[0, gi] = res[:half]
        for g, o_ref in enumerate(other_refs):
            @pl.when(j == g)
            def _():
                o_ref[gi] = res[half:]


def gate_up(tokens, gq, gs, uq, us):
    rows, k = tokens.shape
    cols = gq.shape[1]
    tn = cols // GROUPS
    hr = rows // 2
    gsr = jnp.repeat(gs, BLK, axis=1)
    usr = jnp.repeat(us, BLK, axis=1)
    if not USE_PALLAS:
        def deq(q, sr):
            return (q.astype(jnp.float32) * jnp.repeat(sr, BLK, axis=0)).astype(jnp.bfloat16)
        g = jnp.dot(tokens, deq(gq, gsr), preferred_element_type=jnp.float32).astype(jnp.bfloat16)
        u = jnp.dot(tokens, deq(uq, usr), preferred_element_type=jnp.float32).astype(jnp.bfloat16)
        both = jnp.stack([g, u])
        both = both.reshape(2, 2, hr, GROUPS, tn).transpose(1, 3, 0, 2, 4)
        return [both[0]] + [both[1, g] for g in range(GROUPS)]
    nb = k // BLK
    return pl.pallas_call(
        gate_up_kernel,
        grid=(GROUPS,),
        in_specs=[
            pl.BlockSpec((rows, k), lambda j: (0, 0)),
            pl.BlockSpec((k, tn), lambda j: (0, j)),
            pl.BlockSpec((nb, tn), lambda j: (0, j)),
            pl.BlockSpec((k, tn), lambda j: (0, j)),
            pl.BlockSpec((nb, tn), lambda j: (0, j)),
        ],
        out_specs=[pl.BlockSpec((1, 2, hr, tn), lambda j: (j, 0, 0, 0))]
        + [pl.BlockSpec((2, hr, tn), lambda j: (0, 0, 0))] * GROUPS,
        out_shape=[jax.ShapeDtypeStruct((GROUPS, 2, hr, tn), jnp.bfloat16)]
        + [jax.ShapeDtypeStruct((2, hr, tn), jnp.bfloat16)] * GROUPS,
        compiler_params=pltpu.CompilerParams(vmem_limit_bytes=48 * 1024 * 1024),
    )(tokens, gq, gsr, uq, usr)


def down_kernel(q_ref, s_ref, *refs):
    h_refs, o_ref = refs[:-1], refs[-1]
    k = pl.program_id(0)
    tk = q_ref.shape[0]
    nb = tk // BLK

    @pl.when(k == 0)
    def _():
        o_ref[...] = jnp.zeros_like(o_ref)

    parts = []
    for b in range(nb):
        qb = q_ref[b * BLK:(b + 1) * BLK, :].astype(jnp.float32)
        sb = s_ref[pl.ds(k * nb + b, 1), :]
        parts.append((qb * sb).astype(jnp.bfloat16))
    w = jnp.concatenate(parts, axis=0)
    for g, h_ref in enumerate(h_refs):
        @pl.when(k == g)
        def _():
            o_ref[...] += jnp.dot(h_ref[...], w, preferred_element_type=jnp.float32)


def down(hidden, dq, dsr):
    groups = len(hidden)
    rows, tk = hidden[0].shape
    cols = dq.shape[1]
    if not USE_PALLAS:
        w = (dq.astype(jnp.float32) * jnp.repeat(dsr, BLK, axis=0)).astype(jnp.bfloat16)
        return jnp.dot(jnp.concatenate(hidden, axis=1), w, preferred_element_type=jnp.float32)
    return pl.pallas_call(
        down_kernel,
        grid=(groups,),
        in_specs=[
            pl.BlockSpec((tk, cols), lambda k: (k, 0)),
            pl.BlockSpec(dsr.shape, lambda k: (0, 0)),
        ]
        + [pl.BlockSpec((rows, tk), lambda k: (0, 0))] * groups,
        out_specs=pl.BlockSpec((rows, cols), lambda k: (0, 0)),
        out_shape=jax.ShapeDtypeStruct((rows, cols), jnp.float32),
    )(dq, dsr, *hidden)


def hid_sum(pout, n_hid):
    pb = pout.astype(jnp.bfloat16)
    from_minus = lax.ppermute(pb, "hid", perm_hid(n_hid, 1))
    from_plus = lax.ppermute(pb, "hid", perm_hid(n_hid, -1))
    hr = pout.shape[0] // 2
    fwd_a = lax.ppermute(from_minus[:hr], "hid", perm_hid(n_hid, 1))
    fwd_b = lax.ppermute(from_plus[hr:], "hid", perm_hid(n_hid, -1))
    far = jnp.concatenate([fwd_a, fwd_b], axis=0).astype(jnp.float32)
    return pout + from_minus.astype(jnp.float32) + from_plus.astype(jnp.float32) + far


def shards(n_hid, tokens, gate_quant, gate_scale, up_quant, up_scale, down_quant, down_scale):
    w = lax.axis_index("wid")
    c = w % NC
    x = (w // NC) % NX
    z = w // (NC * NX)
    rows = tokens.shape[0]
    hr = rows // 2

    tok = jnp.concatenate([tokens, tokens], axis=0)
    tok = lax.dynamic_slice_in_dim(tok, c * hr, rows, 0)
    mine, *others = gate_up(tok, gate_quant, gate_scale, up_quant, up_scale)

    pc = perm_core()
    hmine, hother = [], []
    for gi in range(GROUPS):
        recv = lax.ppermute(others[gi], "wid", pc)
        q = mine[gi].astype(jnp.float32) + recv.astype(jnp.float32)
        d = 1 if gi % 2 == 0 else -1
        if gi < 2:
            r1 = ring_rs(q, 1, x, perm_x(d), d, NX)
            r2 = ring_rs(r1, 1, z, perm_z(d), d, NZ)
        else:
            r1 = ring_rs(q, 1, z, perm_z(d), d, NZ)
            r2 = ring_rs(r1, 1, x, perm_x(d), d, NX)
        hg = (jax.nn.silu(r2[0]) * r2[1]).astype(jnp.bfloat16)
        if gi < 2:
            a1 = ring_ag(hg, z, perm_z(d), d, NZ)
            a2 = ring_ag(a1, x, perm_x(d), d, NX)
        else:
            a1 = ring_ag(hg, x, perm_x(d), d, NX)
            a2 = ring_ag(a1, z, perm_z(d), d, NZ)
        hmine.append(a2)
        hother.append(lax.ppermute(a2, "wid", pc))

    dsr = jnp.repeat(down_scale, BLK, axis=1)
    p_mine = down(hmine, down_quant, dsr)
    s_mine = hid_sum(p_mine, n_hid)
    p_other = down(hother, down_quant, dsr)
    s_other = hid_sum(p_other, n_hid)
    rolled = jnp.concatenate([s_mine, s_other, s_mine], axis=0).astype(jnp.bfloat16)
    return lax.dynamic_slice_in_dim(rolled, c * hr, rows, 0)


def solution(mesh):
    n_hid = mesh.shape["hid"]
    assert n_hid == 4 and mesh.shape["wid"] == NZ * NX * NC
    return jax.shard_map(
        functools.partial(shards, n_hid),
        mesh=mesh,
        in_specs=(
            P(None, "wid"),
            P("wid", "hid"),
            P("wid", "hid"),
            P("wid", "hid"),
            P("wid", "hid"),
            P("hid", "wid"),
            P("hid", "wid"),
        ),
        out_specs=P(None, "wid"),
        check_vma=False,
    )
```
